32 devices in a mesh: grp: 2 (over x), dec: 16 (over z, y, core).
Axes of the slice: x: 2, y: 2, z: 4, core: 2. Of those that a mesh axis runs over, the one named last changes fastest.
Arguments:
- latents: bfloat16 [4096, 4, 512], P(('grp', 'dec')), parts along dimension 0, may hold values from -6 to 6
- cache: bfloat16 [4096, 7, 512], P(('grp', 'dec')), parts along dimension 0, may hold values from -6 to 6
- panel_slot: int32 [4096], P(('grp', 'dec')), parts along dimension 0, may hold values from 0 to 2047, as said below
- cache_slot: int32 [4096], P(('grp', 'dec')), parts along dimension 0, may hold values from 0 to 2047, as said below
- frames_valid: int32 [4096], P(('grp', 'dec')), parts along dimension 0, may hold values from 1 to 4
- up_weight: float32 [4, 512], replicated, may hold values from -3 to 3
- conv_weight: bfloat16 [7, 512, 1024], replicated, may hold values from -0.09375 to 0.09375
- conv_bias: float32 [1024], replicated, may hold values from -0.5 to 0.5
Outputs:
- decoded: bfloat16 [4096, 8, 1024], P(('grp', 'dec')), parts along dimension 0
- new_cache: bfloat16 [4096, 7, 512], P(('grp', 'dec')), parts along dimension 0
The draws below stay inside these ranges and needn't reach their ends.
There are 2 independent parts, one for each index of `grp`. The reference program is written for one: setup_inputs(seed, part) draws one part's arguments, and reference() takes and returns one part's arrays. A program takes and returns all parts, laid end to end along the dimension named above; an argument that names none is the same for every part. Nothing has to cross between parts.
Inputs may be any that keep to these rules, and one draw needn't show every extreme that they name: `panel_slot`: A permutation of the owner slots. Each device's rows go to owner devices in the same counts; at most 9 rows of one device go to one owner device, and every device has one owner device that receives exactly 9 of its rows. `cache_slot`: A permutation of the owner slots. Exactly 64 of each device's slots go to other devices, the rest keep their slot; at most 5 go from one device to one other device, and every device sends exactly 5 to one of them.
All inputs are finite; a program needn't handle non-finite values.
Results may differ from the reference program's by a relative error of at most 0.0034.
Values may be sent and summed in bfloat16 or wider, within the bound.
No kernel may reach another device: no remote copies, remote signals or barrier semaphores. Data moves between devices by JAX's collectives and lax.ppermute only.
A program may use at most 64 MiB of HBM per device.

```python
import jax
import jax.numpy as jnp

C = 512
CH = 1024
FRAMES = 4
KSIZE = 7
NCACHE = 7
S_DEV = 128
MIG_DEV = 64
PAIR_CAP = 9
MIG_CAP = 5
STREAMS = 2048
N_DEC = 16


def offsets_with_peak(key, count, peak, number, skip_zero):
    start = 1 if skip_zero else 0
    order = jax.random.permutation(key, number - start) + start
    others = order[1:]
    repeats = (count - peak) // others.shape[0] + 1
    tiled = jnp.tile(others, repeats)[:count - peak]
    return jnp.concatenate([jnp.full((peak,), order[0], jnp.int32), tiled.astype(jnp.int32)])


def device_perms(key, rows, size):
    keys = jax.random.split(key, rows)
    return jax.vmap(lambda one: jax.random.permutation(one, size))(keys).astype(jnp.int32)


def relabel(key, number):
    forward = jax.random.permutation(key, number).astype(jnp.int32)
    backward = jnp.argsort(forward, stable=True).astype(jnp.int32)
    return (forward, backward)


def draw_panel_slot(key, part):
    number = N_DEC
    offsets = offsets_with_peak(jax.random.fold_in(key, 11), S_DEV, PAIR_CAP, number, False)
    forward, backward = relabel(jax.random.fold_in(key, 12), number)
    rows = device_perms(jax.random.fold_in(key, 13), number, S_DEV)
    places = device_perms(jax.random.fold_in(key, 14), number, S_DEV)
    source = jnp.arange(number, dtype=jnp.int32)[:, None]
    which = rows
    target = backward[(forward[source] + offsets[which]) % number]
    local = places[target, which]
    return (target * S_DEV + local).reshape(-1).astype(jnp.int32)


def draw_cache_slot(key, part):
    number = N_DEC
    offsets = offsets_with_peak(jax.random.fold_in(key, 21), MIG_DEV, MIG_CAP, number, True)
    forward, backward = relabel(jax.random.fold_in(key, 22), number)
    orders = device_perms(jax.random.fold_in(key, 23), number, S_DEV)
    ranks = jnp.argsort(orders, axis=1, stable=True).astype(jnp.int32)
    places = device_perms(jax.random.fold_in(key, 24), number, MIG_DEV)
    source = jnp.arange(number, dtype=jnp.int32)[:, None]
    slot = jnp.arange(S_DEV, dtype=jnp.int32)[None, :]
    moving = ranks < MIG_DEV
    which = jnp.minimum(ranks, MIG_DEV - 1)
    target = backward[(forward[source] + offsets[which]) % number]
    vacated = orders[target, places[target, which]]
    device_of = jnp.where(moving, target, source)
    local = jnp.where(moving, vacated, slot)
    return (device_of * S_DEV + local).reshape(-1).astype(jnp.int32)


def with_ends(result, rng, smallest, high):
    place = [jax.random.randint(jax.random.fold_in(rng, axis), (), 0, length) for axis, length in enumerate(result.shape)]
    longest = result.shape.index(max(result.shape))
    beside = place[:longest] + [(place[longest] + 1) % result.shape[longest]] + place[longest + 1:]
    return result.at[tuple(place)].set(smallest).at[tuple(beside)].set(high)


def block_scale(own_key, extent, cuts, low, largest):
    def one(dim, parts):
        heights = jax.random.uniform(jax.random.fold_in(jax.random.fold_in(own_key, 6), dim), (parts,), jnp.float32, low / len(cuts), largest / len(cuts))
        return jnp.repeat(jnp.exp(heights), extent[dim] // parts).reshape((-1,) + (1,) * (len(extent) - dim - 1))

    loudness = one(*cuts[0])
    for cut in cuts[1:]:
        loudness = loudness * one(*cut)
    return loudness


def normal_values(own_key, dims, spread, bound, cuts=(), kind=jnp.bfloat16):
    values = jax.random.normal(own_key, dims, jnp.float32) * spread
    if len(cuts) > 0:
        values = block_scale(own_key, dims, cuts, -0.22, 0.18) * values
    return jnp.clip(values, min=-bound, max=bound).astype(kind)


def setup_inputs(seed: int = 0, part: int = 0) -> dict:
    streams_of = jax.random.split(jax.random.key(seed), 9)
    own_keys = jax.random.split(jax.random.fold_in(streams_of[8], part), 9)
    return {
        "latents": normal_values(own_keys[0], (STREAMS, FRAMES, C), 1.0, 6.0, ((0, 16),)),
        "cache": normal_values(own_keys[1], (STREAMS, NCACHE, C), 1.0, 6.0, ((0, 16),)),
        "panel_slot": draw_panel_slot(jax.random.fold_in(jax.random.fold_in(streams_of[8], part), 71), part),
        "cache_slot": draw_cache_slot(jax.random.fold_in(jax.random.fold_in(streams_of[8], part), 71), part),
        "frames_valid": with_ends(jax.random.randint(own_keys[4], (STREAMS,), 1, FRAMES + 1), jax.random.fold_in(own_keys[4], 1), 1, FRAMES).astype(jnp.int32),
        "up_weight": normal_values(streams_of[5], (4, C), 0.5, 3.0, (), jnp.float32),
        "conv_weight": normal_values(streams_of[6], (KSIZE, C, CH), (KSIZE * C) ** -0.5, 0.09375),
        "conv_bias": jnp.clip(jax.random.uniform(streams_of[7], (CH,), jnp.float32, -0.5, 0.5), -0.5, 0.5),
    }


def reference(latents, cache, panel_slot, cache_slot, frames_valid, up_weight, conv_weight, conv_bias):
    panels = jnp.zeros_like(latents).at[panel_slot].set(latents)
    owned = jnp.zeros_like(cache).at[cache_slot].set(cache)
    prev = jnp.concatenate([owned[:, 0:1], panels], axis=1)
    current = prev[:, 1:].astype(jnp.float32)
    past = prev[:, :-1].astype(jnp.float32)
    even = up_weight[0] * current + up_weight[2] * past
    odd = up_weight[1] * current + up_weight[3] * past
    count = latents.shape[0]
    upsampled = jnp.stack([even, odd], axis=2).reshape(count, 2 * FRAMES, C).astype(jnp.bfloat16)
    extended = jnp.concatenate([owned[:, 1:], upsampled], axis=1)
    total = jnp.zeros((count * 2 * FRAMES, CH), jnp.float32) + conv_bias
    for tap in range(KSIZE):
        window = extended[:, tap:tap + 2 * FRAMES].reshape(count * 2 * FRAMES, C)
        total = total + jnp.dot(window, conv_weight[tap], preferred_element_type=jnp.float32)
    active = jax.nn.elu(total).reshape(count, 2 * FRAMES, CH)
    position = jnp.arange(2 * FRAMES, dtype=jnp.int32)
    keep = position[None, :] < 2 * frames_valid[:, None]
    decoded = jnp.where(keep[:, :, None], active, 0.0).astype(jnp.bfloat16)
    pick_latent = (jnp.arange(FRAMES + 1, dtype=jnp.int32)[None, :] == frames_valid[:, None]).astype(jnp.float32)
    last_latent = jnp.einsum("sf,sfc->sc", pick_latent, prev.astype(jnp.float32))
    target = 2 * frames_valid[:, None, None] + jnp.arange(KSIZE - 1, dtype=jnp.int32)[None, :, None]
    pick_rows = (jnp.arange(KSIZE - 1 + 2 * FRAMES, dtype=jnp.int32)[None, None, :] == target).astype(jnp.float32)
    last_rows = jnp.einsum("sjt,stc->sjc", pick_rows, extended.astype(jnp.float32))
    new_cache = jnp.concatenate([last_latent[:, None], last_rows], axis=1).astype(jnp.bfloat16)
    return decoded, new_cache
```

```python
import jax
import jax.numpy as jnp
from jax import lax
from jax.experimental import pallas as pl
from jax.experimental.pallas import tpu as pltpu
from jax.sharding import PartitionSpec as P


LABEL_WIDTH = 128


def buckets(rows, target, local, capacity, number):
    hits = (target[:, None] == jnp.arange(number, dtype=jnp.int32)[None, :]).astype(jnp.int32)
    rank = jnp.sum(hits * (jnp.cumsum(hits, axis=0) - 1), axis=1)
    place = jnp.where(target >= 0, target * capacity + rank, -1)
    picker = (place[:, None] == jnp.arange(number * capacity, dtype=jnp.int32)[None, :]).astype(
        jnp.bfloat16
    )
    packed = jnp.dot(picker.T, rows, preferred_element_type=jnp.float32).astype(jnp.bfloat16)
    labels = (
        jnp.sum(picker.T.astype(jnp.float32) * (local + 1).astype(jnp.float32)[None, :], axis=1)
        - 1.0
    )
    width = rows.shape[1]
    return (
        packed.reshape(number, capacity * width),
        labels.reshape(number, capacity),
    )


def settle(received, labels, streams):
    picker = (labels[:, None] == jnp.arange(streams, dtype=jnp.float32)[None, :]).astype(
        jnp.bfloat16
    )
    return jnp.dot(picker.T, received, preferred_element_type=jnp.float32)


def conv_kernel(ext_ref, w_ref, b_ref, lim_ref, o_ref):
    taps = w_ref.shape[0]
    steps, streams, block = o_ref.shape
    channels = ext_ref.shape[2]
    acc = None
    for tap in range(taps):
        window = ext_ref[tap : tap + steps].reshape(steps * streams, channels)
        part = jnp.dot(window, w_ref[tap], preferred_element_type=jnp.float32)
        acc = part if acc is None else acc + part
    acc = acc + b_ref[...]
    act = jnp.where(acc > 0, acc, jnp.exp(jnp.minimum(acc, 0.0)) - 1.0)
    act = act.reshape(steps, streams, block)
    lim = lim_ref[...]
    for step in range(steps):
        keep = step < lim
        o_ref[step] = jnp.where(keep, act[step], 0.0).astype(o_ref.dtype)


def conv_call(ext_t, conv_weight, conv_bias, limit, steps):
    rows, streams, channels = ext_t.shape
    taps, _, outward = conv_weight.shape
    block = 256 if outward % 256 == 0 else outward
    return pl.pallas_call(
        conv_kernel,
        out_shape=jax.ShapeDtypeStruct((steps, streams, outward), jnp.bfloat16),
        grid=(outward // block,),
        in_specs=[
            pl.BlockSpec((rows, streams, channels), lambda n: (0, 0, 0)),
            pl.BlockSpec((taps, channels, block), lambda n: (0, 0, n)),
            pl.BlockSpec((1, block), lambda n: (0, n)),
            pl.BlockSpec((streams, 1), lambda n: (0, 0)),
        ],
        out_specs=pl.BlockSpec((steps, streams, block), lambda n: (0, 0, n)),
    )(ext_t, conv_weight, conv_bias.reshape(1, outward), limit)


def body(latents, cache, panel_slot, cache_slot, frames_valid, up_weight, conv_weight, conv_bias):
    number = lax.axis_size("dec")
    myself = lax.axis_index("dec")
    streams = latents.shape[0]
    frames = latents.shape[1]
    channels = latents.shape[2]
    rows_kept = cache.shape[1]
    pair_cap = max(2, (streams + number - 2) // (number - 1))
    mig_cap = max(2, (streams // 2 + number - 3) // (number - 2))
    panel_width = frames * channels
    cache_width = rows_kept * channels
    flat_latents = latents.reshape(streams, panel_width)
    flat_cache = cache.reshape(streams, cache_width)
    panel_owner = panel_slot // streams
    panel_local = panel_slot % streams
    cache_owner = cache_slot // streams
    cache_local = cache_slot % streams
    moving = cache_owner != myself
    staying = jnp.logical_not(moving)
    stay_pick = (
        staying[:, None] & (cache_local[:, None] == jnp.arange(streams, dtype=jnp.int32)[None, :])
    ).astype(jnp.bfloat16)
    kept = jnp.dot(stay_pick.T, flat_cache, preferred_element_type=jnp.float32)
    cache_send, cache_labels = buckets(
        flat_cache, jnp.where(moving, cache_owner, -1), cache_local, mig_cap, number
    )
    panel_send, panel_labels = buckets(flat_latents, panel_owner, panel_local, pair_cap, number)
    label_block = jnp.concatenate([panel_labels, cache_labels], axis=1)
    label_block = jnp.pad(
        label_block, ((0, 0), (0, LABEL_WIDTH - label_block.shape[1])), constant_values=-1.0
    ).astype(jnp.bfloat16)
    joint = jnp.concatenate([panel_send, cache_send, label_block], axis=1)
    joint_recv = lax.all_to_all(joint, "dec", split_axis=0, concat_axis=0, tiled=True)
    split_at = pair_cap * panel_width
    label_at = split_at + mig_cap * cache_width
    panel_recv = joint_recv[:, :split_at].reshape(number * pair_cap, panel_width)
    cache_recv = joint_recv[:, split_at:label_at].reshape(number * mig_cap, cache_width)
    recv_labels = joint_recv[:, label_at:].astype(jnp.float32)
    panel_rl = recv_labels[:, :pair_cap].reshape(-1)
    cache_rl = recv_labels[:, pair_cap : pair_cap + mig_cap].reshape(-1)
    panels = settle(panel_recv, panel_rl, streams)
    arrived = settle(cache_recv, cache_rl, streams)
    latent_rows = panels.astype(jnp.bfloat16).reshape(streams, frames, channels)
    owned = (kept + arrived).astype(jnp.bfloat16).reshape(streams, rows_kept, channels)
    previous = jnp.concatenate([owned[:, 0:1], latent_rows], axis=1)
    previous_t = jnp.transpose(previous, (1, 0, 2))
    current = previous_t[1:].astype(jnp.float32)
    earlier = previous_t[:-1].astype(jnp.float32)
    even = up_weight[0] * current + up_weight[2] * earlier
    odd = up_weight[1] * current + up_weight[3] * earlier
    upsampled_t = (
        jnp.stack([even, odd], axis=1).reshape(2 * frames, streams, channels).astype(jnp.bfloat16)
    )
    owned_t = jnp.transpose(owned[:, 1:], (1, 0, 2))
    extended_t = jnp.concatenate([owned_t, upsampled_t], axis=0)
    limit = (2 * frames_valid).reshape(streams, 1)
    decoded_t = conv_call(extended_t, conv_weight, conv_bias, limit, 2 * frames)
    decoded = jnp.transpose(decoded_t, (1, 0, 2))
    taps = conv_weight.shape[0]
    last_latent = previous[:, 1]
    last_rows = extended_t[2 : 2 + taps - 1]
    for valid in range(2, frames + 1):
        chosen = frames_valid == valid
        last_latent = jnp.where(chosen[:, None], previous[:, valid], last_latent)
        last_rows = jnp.where(
            chosen[None, :, None], extended_t[2 * valid : 2 * valid + taps - 1], last_rows
        )
    new_cache = jnp.concatenate(
        [last_latent[:, None], jnp.transpose(last_rows, (1, 0, 2))], axis=1
    )
    return (decoded, new_cache)


def solution(mesh):
    in_specs = (
        P(("grp", "dec"), None, None),
        P(("grp", "dec"), None, None),
        P(("grp", "dec")),
        P(("grp", "dec")),
        P(("grp", "dec")),
        P(),
        P(),
        P(),
    )
    out_specs = (P(("grp", "dec"), None, None), P(("grp", "dec"), None, None))
    return jax.shard_map(body, mesh=mesh, in_specs=in_specs, out_specs=out_specs, check_vma=False)
```

```python
import functools

import jax
import jax.numpy as jnp
from jax import lax
from jax.experimental import pallas as pl
from jax.experimental.pallas import tpu as pltpu
from jax.sharding import PartitionSpec as P


LABEL_WIDTH = 128


def buckets(rows, target, local, capacity, number):
    hits = (target[:, None] == jnp.arange(number, dtype=jnp.int32)[None, :]).astype(jnp.int32)
    rank = jnp.sum(hits * (jnp.cumsum(hits, axis=0) - 1), axis=1)
    place = jnp.where(target >= 0, target * capacity + rank, -1)
    picker = (place[:, None] == jnp.arange(number * capacity, dtype=jnp.int32)[None, :]).astype(
        jnp.bfloat16
    )
    packed = jnp.dot(picker.T, rows, preferred_element_type=jnp.float32).astype(jnp.bfloat16)
    labels = (
        jnp.sum(picker.T.astype(jnp.float32) * (local + 1).astype(jnp.float32)[None, :], axis=1)
        - 1.0
    )
    width = rows.shape[1]
    return (
        packed.reshape(number, capacity * width),
        labels.reshape(number, capacity),
    )


def settle(received, labels, streams):
    picker = (labels[:, None] == jnp.arange(streams, dtype=jnp.float32)[None, :]).astype(
        jnp.bfloat16
    )
    return jnp.einsum("ps,pqc->sqc", picker, received, preferred_element_type=jnp.float32)


def conv_kernel(ext_ref, w_ref, b_ref, lim_ref, o_ref, *, group):
    taps = w_ref.shape[0]
    streams, steps, block = o_ref.shape
    channels = ext_ref.shape[2]
    rows = steps * group
    line = lax.broadcasted_iota(jnp.int32, (rows, rows), 0)
    column = lax.broadcasted_iota(jnp.int32, (rows, rows), 1)
    order = ((line // steps) == (column % group)) & ((line % steps) == (column // group))
    order = order.astype(jnp.bfloat16)
    position = lax.broadcasted_iota(jnp.int32, (steps, group, 1), 0)
    for first in range(0, streams, group):
        acc = None
        for tap in range(taps):
            window = ext_ref[tap : tap + steps, first : first + group, :].reshape(rows, channels)
            part = jnp.dot(window, w_ref[tap], preferred_element_type=jnp.float32)
            acc = part if acc is None else acc + part
        acc = acc + b_ref[...]
        act = jnp.where(acc > 0, acc, jnp.exp(jnp.minimum(acc, 0.0)) - 1.0)
        act = act.reshape(steps, group, block)
        keep = position < lim_ref[first : first + group, :][None]
        act = jnp.where(keep, act, 0.0).astype(jnp.bfloat16).reshape(rows, block)
        moved = jnp.dot(order, act, preferred_element_type=jnp.float32)
        o_ref[first : first + group] = moved.reshape(group, steps, block).astype(o_ref.dtype)


def conv_call(ext_t, conv_weight, conv_bias, limit, steps):
    rows, streams, channels = ext_t.shape
    taps, _, outward = conv_weight.shape
    block = 256 if outward % 256 == 0 else outward
    group = 32 if streams % 32 == 0 else streams
    return pl.pallas_call(
        functools.partial(conv_kernel, group=group),
        out_shape=jax.ShapeDtypeStruct((streams, steps, outward), jnp.bfloat16),
        grid=(outward // block,),
        in_specs=[
            pl.BlockSpec((rows, streams, channels), lambda n: (0, 0, 0)),
            pl.BlockSpec((taps, channels, block), lambda n: (0, 0, n)),
            pl.BlockSpec((1, block), lambda n: (0, n)),
            pl.BlockSpec((streams, 1), lambda n: (0, 0)),
        ],
        out_specs=pl.BlockSpec((streams, steps, block), lambda n: (0, 0, n)),
    )(ext_t, conv_weight, conv_bias.reshape(1, outward), limit)


def body(latents, cache, panel_slot, cache_slot, frames_valid, up_weight, conv_weight, conv_bias):
    number = lax.axis_size("dec")
    myself = lax.axis_index("dec")
    streams = latents.shape[0]
    frames = latents.shape[1]
    channels = latents.shape[2]
    rows_kept = cache.shape[1]
    pair_cap = max(2, (streams + number - 2) // (number - 1))
    mig_cap = max(2, (streams // 2 + number - 3) // (number - 2))
    panel_width = frames * channels
    cache_width = rows_kept * channels
    flat_latents = latents.reshape(streams, panel_width)
    flat_cache = cache.reshape(streams, cache_width)
    panel_owner = panel_slot // streams
    panel_local = panel_slot % streams
    cache_owner = cache_slot // streams
    cache_local = cache_slot % streams
    moving = cache_owner != myself
    staying = jnp.logical_not(moving)
    stay_pick = (
        staying[:, None] & (cache_local[:, None] == jnp.arange(streams, dtype=jnp.int32)[None, :])
    ).astype(jnp.bfloat16)
    kept = jnp.dot(stay_pick.T, flat_cache, preferred_element_type=jnp.float32)
    cache_send, cache_labels = buckets(
        flat_cache, jnp.where(moving, cache_owner, -1), cache_local, mig_cap, number
    )
    panel_send, panel_labels = buckets(flat_latents, panel_owner, panel_local, pair_cap, number)
    lane = LABEL_WIDTH
    panel_rows = pair_cap * panel_width // lane
    cache_rows = mig_cap * cache_width // lane
    label_rows = -(panel_rows + cache_rows + 1) % 16 + 1
    label_block = jnp.concatenate([panel_labels, cache_labels], axis=1)
    label_block = jnp.pad(
        label_block, ((0, 0), (0, label_rows * lane - label_block.shape[1])), constant_values=-1.0
    ).astype(jnp.bfloat16)
    joint = jnp.concatenate(
        [
            panel_send.reshape(number, panel_rows, lane),
            cache_send.reshape(number, cache_rows, lane),
            label_block.reshape(number, label_rows, lane),
        ],
        axis=1,
    )
    joint_recv = lax.all_to_all(joint, "dec", split_axis=0, concat_axis=0, tiled=True)
    panel_recv = joint_recv[:, :panel_rows].reshape(number * pair_cap, panel_width // lane, lane)
    cache_recv = joint_recv[:, panel_rows : panel_rows + cache_rows].reshape(
        number * mig_cap, cache_width // lane, lane
    )
    recv_labels = joint_recv[:, panel_rows + cache_rows, :].astype(jnp.float32)
    panel_rl = recv_labels[:, :pair_cap].reshape(-1)
    cache_rl = recv_labels[:, pair_cap : pair_cap + mig_cap].reshape(-1)
    panels = settle(panel_recv, panel_rl, streams).reshape(streams, panel_width)
    arrived = settle(cache_recv, cache_rl, streams).reshape(streams, cache_width)
    latent_rows = panels.astype(jnp.bfloat16).reshape(streams, frames, channels)
    owned = (kept + arrived).astype(jnp.bfloat16).reshape(streams, rows_kept, channels)
    previous = jnp.concatenate([owned[:, 0:1], latent_rows], axis=1)
    previous_t = jnp.transpose(previous, (1, 0, 2))
    current = previous_t[1:].astype(jnp.float32)
    earlier = previous_t[:-1].astype(jnp.float32)
    even = up_weight[0] * current + up_weight[2] * earlier
    odd = up_weight[1] * current + up_weight[3] * earlier
    upsampled_t = (
        jnp.stack([even, odd], axis=1).reshape(2 * frames, streams, channels).astype(jnp.bfloat16)
    )
    owned_t = jnp.transpose(owned[:, 1:], (1, 0, 2))
    extended_t = jnp.concatenate([owned_t, upsampled_t], axis=0)
    limit = (2 * frames_valid).reshape(streams, 1)
    decoded = conv_call(extended_t, conv_weight, conv_bias, limit, 2 * frames)
    taps = conv_weight.shape[0]
    last_latent = previous[:, 1]
    last_rows = extended_t[2 : 2 + taps - 1]
    for valid in range(2, frames + 1):
        chosen = frames_valid == valid
        last_latent = jnp.where(chosen[:, None], previous[:, valid], last_latent)
        last_rows = jnp.where(
            chosen[None, :, None], extended_t[2 * valid : 2 * valid + taps - 1], last_rows
        )
    new_cache = jnp.concatenate(
        [last_latent[:, None], jnp.transpose(last_rows, (1, 0, 2))], axis=1
    )
    return (decoded, new_cache)


def solution(mesh):
    in_specs = (
        P(("grp", "dec"), None, None),
        P(("grp", "dec"), None, None),
        P(("grp", "dec")),
        P(("grp", "dec")),
        P(("grp", "dec")),
        P(),
        P(),
        P(),
    )
    out_specs = (P(("grp", "dec"), None, None), P(("grp", "dec"), None, None))
    return jax.shard_map(body, mesh=mesh, in_specs=in_specs, out_specs=out_specs, check_vma=False)
```

```python
import jax
import jax.numpy as jnp
from jax import lax
from jax.experimental import pallas as pl
from jax.experimental.pallas import tpu as pltpu
from jax.sharding import PartitionSpec as P


LABEL_WIDTH = 128


def buckets(rows, target, local, capacity, number):
    hits = (target[:, None] == jnp.arange(number, dtype=jnp.int32)[None, :]).astype(jnp.int32)
    rank = jnp.sum(hits * (jnp.cumsum(hits, axis=0) - 1), axis=1)
    place = jnp.where(target >= 0, target * capacity + rank, -1)
    picker = (place[:, None] == jnp.arange(number * capacity, dtype=jnp.int32)[None, :]).astype(
        jnp.bfloat16
    )
    packed = jnp.dot(picker.T, rows, preferred_element_type=jnp.float32).astype(jnp.bfloat16)
    labels = (
        jnp.sum(picker.T.astype(jnp.float32) * (local + 1).astype(jnp.float32)[None, :], axis=1)
        - 1.0
    )
    width = rows.shape[1]
    return (
        packed.reshape(number, capacity * width),
        labels.reshape(number, capacity),
    )


def settle(received, labels, streams):
    picker = (labels[:, None] == jnp.arange(streams, dtype=jnp.float32)[None, :]).astype(
        jnp.bfloat16
    )
    return jnp.dot(picker.T, received, preferred_element_type=jnp.float32)


def conv_kernel(own_ref, pan_ref, uw_ref, w_ref, b_ref, lim_ref, o_ref, nc_ref, ext_ref):
    taps = w_ref.shape[0]
    steps, streams, block = o_ref.shape
    rows, _, channels = ext_ref.shape
    kept_rows = own_ref.shape[1] // channels
    frames = pan_ref.shape[1] // channels
    lim = lim_ref[...]

    @pl.when(pl.program_id(0) == 0)
    def _():
        prev = [own_ref[:, 0:channels]] + [
            pan_ref[:, f * channels : (f + 1) * channels] for f in range(frames)
        ]
        for row in range(kept_rows - 1):
            ext_ref[row] = own_ref[:, (row + 1) * channels : (row + 2) * channels]
        weight = uw_ref[...]
        for f in range(frames):
            current = prev[f + 1].astype(jnp.float32)
            earlier = prev[f].astype(jnp.float32)
            for j in range(2):
                value = weight[j : j + 1] * current + weight[j + 2 : j + 3] * earlier
                ext_ref[kept_rows - 1 + 2 * f + j] = value.astype(ext_ref.dtype)
        first = prev[1]
        tail = [ext_ref[2 + i] for i in range(kept_rows - 1)]
        for valid in range(2, frames + 1):
            chosen = lim == 2 * valid
            first = jnp.where(chosen, prev[valid], first)
            tail = [
                jnp.where(chosen, ext_ref[2 * valid + i], tail[i]) for i in range(kept_rows - 1)
            ]
        nc_ref[:, 0:channels] = first
        for i in range(kept_rows - 1):
            nc_ref[:, (i + 1) * channels : (i + 2) * channels] = tail[i]

    acc = None
    for tap in range(taps):
        window = ext_ref[tap : tap + steps].reshape(steps * streams, channels)
        part = jnp.dot(window, w_ref[tap], preferred_element_type=jnp.float32)
        acc = part if acc is None else acc + part
    acc = acc + b_ref[...]
    act = jnp.where(acc > 0, acc, jnp.exp(jnp.minimum(acc, 0.0)) - 1.0)
    act = act.reshape(steps, streams, block)
    for step in range(steps):
        o_ref[step] = jnp.where(step < lim, act[step], 0.0).astype(o_ref.dtype)


def conv_call(owned, panels, up_weight, conv_weight, conv_bias, limit, steps):
    streams, cache_width = owned.shape
    panel_width = panels.shape[1]
    taps, channels, outward = conv_weight.shape
    rows = cache_width // channels - 1 + steps
    block = 256 if outward % 256 == 0 else outward
    whole = lambda n: (0, 0)
    return pl.pallas_call(
        conv_kernel,
        out_shape=(
            jax.ShapeDtypeStruct((steps, streams, outward), jnp.bfloat16),
            jax.ShapeDtypeStruct((streams, cache_width), jnp.bfloat16),
        ),
        grid=(outward // block,),
        in_specs=[
            pl.BlockSpec((streams, cache_width), whole),
            pl.BlockSpec((streams, panel_width), whole),
            pl.BlockSpec(up_weight.shape, whole),
            pl.BlockSpec((taps, channels, block), lambda n: (0, 0, n)),
            pl.BlockSpec((1, block), lambda n: (0, n)),
            pl.BlockSpec((streams, 1), whole),
        ],
        out_specs=(
            pl.BlockSpec((steps, streams, block), lambda n: (0, 0, n)),
            pl.BlockSpec((streams, cache_width), whole),
        ),
        scratch_shapes=[pltpu.VMEM((rows, streams, channels), jnp.bfloat16)],
        compiler_params=pltpu.CompilerParams(dimension_semantics=("arbitrary",)),
    )(owned, panels, up_weight, conv_weight, conv_bias.reshape(1, outward), limit)


def body(latents, cache, panel_slot, cache_slot, frames_valid, up_weight, conv_weight, conv_bias):
    number = lax.axis_size("dec")
    myself = lax.axis_index("dec")
    streams = latents.shape[0]
    frames = latents.shape[1]
    channels = latents.shape[2]
    rows_kept = cache.shape[1]
    pair_cap = max(2, (streams + number - 2) // (number - 1))
    mig_cap = max(2, (streams // 2 + number - 3) // (number - 2))
    panel_width = frames * channels
    cache_width = rows_kept * channels
    flat_latents = latents.reshape(streams, panel_width)
    flat_cache = cache.reshape(streams, cache_width)
    panel_owner = panel_slot // streams
    panel_local = panel_slot % streams
    cache_owner = cache_slot // streams
    cache_local = cache_slot % streams
    moving = cache_owner != myself
    staying = jnp.logical_not(moving)
    stay_pick = (
        staying[:, None] & (cache_local[:, None] == jnp.arange(streams, dtype=jnp.int32)[None, :])
    ).astype(jnp.bfloat16)
    kept = jnp.dot(stay_pick.T, flat_cache, preferred_element_type=jnp.float32)
    cache_send, cache_labels = buckets(
        flat_cache, jnp.where(moving, cache_owner, -1), cache_local, mig_cap, number
    )
    panel_send, panel_labels = buckets(flat_latents, panel_owner, panel_local, pair_cap, number)
    lane = LABEL_WIDTH
    panel_rows = pair_cap * panel_width // lane
    cache_rows = mig_cap * cache_width // lane
    label_rows = -(panel_rows + cache_rows + 1) % 16 + 1
    label_block = jnp.concatenate([panel_labels, cache_labels], axis=1)
    label_block = jnp.pad(
        label_block, ((0, 0), (0, label_rows * lane - label_block.shape[1])), constant_values=-1.0
    ).astype(jnp.bfloat16)
    joint = jnp.concatenate(
        [
            panel_send.reshape(number, panel_rows, lane),
            cache_send.reshape(number, cache_rows, lane),
            label_block.reshape(number, label_rows, lane),
        ],
        axis=1,
    )
    joint_recv = lax.all_to_all(joint, "dec", split_axis=0, concat_axis=0, tiled=True)
    panel_recv = joint_recv[:, :panel_rows].reshape(number * pair_cap, panel_width)
    cache_recv = joint_recv[:, panel_rows : panel_rows + cache_rows].reshape(
        number * mig_cap, cache_width
    )
    recv_labels = joint_recv[:, panel_rows + cache_rows, :].astype(jnp.float32)
    panel_rl = recv_labels[:, :pair_cap].reshape(-1)
    cache_rl = recv_labels[:, pair_cap : pair_cap + mig_cap].reshape(-1)
    panels = settle(panel_recv, panel_rl, streams).astype(jnp.bfloat16)
    arrived = settle(cache_recv, cache_rl, streams)
    owned = (kept + arrived).astype(jnp.bfloat16)
    limit = (2 * frames_valid).reshape(streams, 1)
    decoded_t, new_cache = conv_call(
        owned, panels, up_weight, conv_weight, conv_bias, limit, 2 * frames
    )
    decoded = jnp.transpose(decoded_t, (1, 0, 2))
    new_cache = new_cache.reshape(streams, rows_kept, channels)
    return (decoded, new_cache)


def solution(mesh):
    in_specs = (
        P(("grp", "dec"), None, None),
        P(("grp", "dec"), None, None),
        P(("grp", "dec")),
        P(("grp", "dec")),
        P(("grp", "dec")),
        P(),
        P(),
        P(),
    )
    out_specs = (P(("grp", "dec"), None, None), P(("grp", "dec"), None, None))
    return jax.shard_map(body, mesh=mesh, in_specs=in_specs, out_specs=out_specs, check_vma=False)
```

```python
import jax
import jax.numpy as jnp
from jax import lax
from jax.experimental import pallas as pl
from jax.experimental.pallas import tpu as pltpu
from jax.sharding import PartitionSpec as P


LABEL_WIDTH = 128


def buckets(rows, target, local, capacity, number):
    hits = (target[:, None] == jnp.arange(number, dtype=jnp.int32)[None, :]).astype(jnp.int32)
    rank = jnp.sum(hits * (jnp.cumsum(hits, axis=0) - 1), axis=1)
    place = jnp.where(target >= 0, target * capacity + rank, -1)
    picker = (place[:, None] == jnp.arange(number * capacity, dtype=jnp.int32)[None, :]).astype(
        jnp.bfloat16
    )
    packed = jnp.dot(picker.T, rows, preferred_element_type=jnp.float32).astype(jnp.bfloat16)
    labels = (
        jnp.sum(picker.T.astype(jnp.float32) * (local + 1).astype(jnp.float32)[None, :], axis=1)
        - 1.0
    )
    width = rows.shape[1]
    return (
        packed.reshape(number, capacity * width),
        labels.reshape(number, capacity),
    )


def settle(received, labels, streams):
    picker = (labels[:, None] == jnp.arange(streams, dtype=jnp.float32)[None, :]).astype(
        jnp.bfloat16
    )
    return jnp.dot(picker.T, received, preferred_element_type=jnp.float32)


def conv_kernel(own_ref, pan_ref, uw_ref, w_ref, b_ref, lim_ref, o_ref, nc_ref, ext_ref):
    taps = w_ref.shape[0]
    streams, steps, block = o_ref.shape
    rows, _, channels = ext_ref.shape
    kept_rows = own_ref.shape[1] // channels
    frames = pan_ref.shape[1] // channels
    lim = lim_ref[...]

    @pl.when(pl.program_id(0) == 0)
    def _():
        prev = [own_ref[:, 0:channels]] + [
            pan_ref[:, f * channels : (f + 1) * channels] for f in range(frames)
        ]
        for row in range(kept_rows - 1):
            ext_ref[row] = own_ref[:, (row + 1) * channels : (row + 2) * channels]
        weight = uw_ref[...]
        for f in range(frames):
            current = prev[f + 1].astype(jnp.float32)
            earlier = prev[f].astype(jnp.float32)
            for j in range(2):
                value = weight[j : j + 1] * current + weight[j + 2 : j + 3] * earlier
                ext_ref[kept_rows - 1 + 2 * f + j] = value.astype(ext_ref.dtype)
        first = prev[1]
        tail = [ext_ref[2 + i] for i in range(kept_rows - 1)]
        for valid in range(2, frames + 1):
            chosen = lim == 2 * valid
            first = jnp.where(chosen, prev[valid], first)
            tail = [
                jnp.where(chosen, ext_ref[2 * valid + i], tail[i]) for i in range(kept_rows - 1)
            ]
        nc_ref[0] = first
        for i in range(kept_rows - 1):
            nc_ref[i + 1] = tail[i]

    acc = None
    for tap in range(taps):
        window = ext_ref[tap : tap + steps].reshape(steps * streams, channels)
        part = jnp.dot(window, w_ref[tap], preferred_element_type=jnp.float32)
        acc = part if acc is None else acc + part
    acc = acc + b_ref[...]
    act = jnp.where(acc > 0, acc, jnp.exp(jnp.minimum(acc, 0.0)) - 1.0)
    act = act.reshape(steps, streams, block)
    for step in range(steps):
        o_ref[:, step, :] = jnp.where(step < lim, act[step], 0.0).astype(o_ref.dtype)


def conv_call(owned, panels, up_weight, conv_weight, conv_bias, limit, steps):
    streams, cache_width = owned.shape
    panel_width = panels.shape[1]
    taps, channels, outward = conv_weight.shape
    rows = cache_width // channels - 1 + steps
    block = 256 if outward % 256 == 0 else outward
    whole = lambda n: (0, 0)
    return pl.pallas_call(
        conv_kernel,
        out_shape=(
            jax.ShapeDtypeStruct((streams, steps, outward), jnp.bfloat16),
            jax.ShapeDtypeStruct((cache_width // channels, streams, channels), jnp.bfloat16),
        ),
        grid=(outward // block,),
        in_specs=[
            pl.BlockSpec((streams, cache_width), whole),
            pl.BlockSpec((streams, panel_width), whole),
            pl.BlockSpec(up_weight.shape, whole),
            pl.BlockSpec((taps, channels, block), lambda n: (0, 0, n)),
            pl.BlockSpec((1, block), lambda n: (0, n)),
            pl.BlockSpec((streams, 1), whole),
        ],
        out_specs=(
            pl.BlockSpec((streams, steps, block), lambda n: (0, 0, n)),
            pl.BlockSpec((cache_width // channels, streams, channels), lambda n: (0, 0, 0)),
        ),
        scratch_shapes=[pltpu.VMEM((rows, streams, channels), jnp.bfloat16)],
        compiler_params=pltpu.CompilerParams(dimension_semantics=("arbitrary",)),
    )(owned, panels, up_weight, conv_weight, conv_bias.reshape(1, outward), limit)


def body(latents, cache, panel_slot, cache_slot, frames_valid, up_weight, conv_weight, conv_bias):
    number = lax.axis_size("dec")
    myself = lax.axis_index("dec")
    streams = latents.shape[0]
    frames = latents.shape[1]
    channels = latents.shape[2]
    rows_kept = cache.shape[1]
    pair_cap = max(2, (streams + number - 2) // (number - 1))
    mig_cap = max(2, (streams // 2 + number - 3) // (number - 2))
    panel_width = frames * channels
    cache_width = rows_kept * channels
    flat_latents = latents.reshape(streams, panel_width)
    flat_cache = cache.reshape(streams, cache_width)
    panel_owner = panel_slot // streams
    panel_local = panel_slot % streams
    cache_owner = cache_slot // streams
    cache_local = cache_slot % streams
    moving = cache_owner != myself
    staying = jnp.logical_not(moving)
    stay_pick = (
        staying[:, None] & (cache_local[:, None] == jnp.arange(streams, dtype=jnp.int32)[None, :])
    ).astype(jnp.bfloat16)
    kept = jnp.dot(stay_pick.T, flat_cache, preferred_element_type=jnp.float32)
    cache_send, cache_labels = buckets(
        flat_cache, jnp.where(moving, cache_owner, -1), cache_local, mig_cap, number
    )
    panel_send, panel_labels = buckets(flat_latents, panel_owner, panel_local, pair_cap, number)
    lane = LABEL_WIDTH
    panel_rows = pair_cap * panel_width // lane
    cache_rows = mig_cap * cache_width // lane
    label_rows = -(panel_rows + cache_rows + 1) % 16 + 1
    label_block = jnp.concatenate([panel_labels, cache_labels], axis=1)
    label_block = jnp.pad(
        label_block, ((0, 0), (0, label_rows * lane - label_block.shape[1])), constant_values=-1.0
    ).astype(jnp.bfloat16)
    joint = jnp.concatenate(
        [
            panel_send.reshape(number, panel_rows, lane),
            cache_send.reshape(number, cache_rows, lane),
            label_block.reshape(number, label_rows, lane),
        ],
        axis=1,
    )
    joint_recv = lax.all_to_all(joint, "dec", split_axis=0, concat_axis=0, tiled=True)
    panel_recv = joint_recv[:, :panel_rows].reshape(number * pair_cap, panel_width)
    cache_recv = joint_recv[:, panel_rows : panel_rows + cache_rows].reshape(
        number * mig_cap, cache_width
    )
    recv_labels = joint_recv[:, panel_rows + cache_rows, :].astype(jnp.float32)
    panel_rl = recv_labels[:, :pair_cap].reshape(-1)
    cache_rl = recv_labels[:, pair_cap : pair_cap + mig_cap].reshape(-1)
    panels = settle(panel_recv, panel_rl, streams).astype(jnp.bfloat16)
    arrived = settle(cache_recv, cache_rl, streams)
    owned = (kept + arrived).astype(jnp.bfloat16)
    limit = (2 * frames_valid).reshape(streams, 1)
    decoded, new_cache = conv_call(
        owned, panels, up_weight, conv_weight, conv_bias, limit, 2 * frames
    )
    new_cache = jnp.transpose(new_cache, (1, 0, 2))
    return (decoded, new_cache)


def solution(mesh):
    in_specs = (
        P(("grp", "dec"), None, None),
        P(("grp", "dec"), None, None),
        P(("grp", "dec")),
        P(("grp", "dec")),
        P(("grp", "dec")),
        P(),
        P(),
        P(),
    )
    out_specs = (P(("grp", "dec"), None, None), P(("grp", "dec"), None, None))
    return jax.shard_map(body, mesh=mesh, in_specs=in_specs, out_specs=out_specs, check_vma=False)
```

```python
import jax
import jax.numpy as jnp
from jax import lax
from jax.experimental import pallas as pl
from jax.experimental.pallas import tpu as pltpu
from jax.sharding import PartitionSpec as P


LABEL_WIDTH = 128


def buckets(rows, target, local, capacity, number):
    hits = (target[:, None] == jnp.arange(number, dtype=jnp.int32)[None, :]).astype(jnp.int32)
    rank = jnp.sum(hits * (jnp.cumsum(hits, axis=0) - 1), axis=1)
    place = jnp.where(target >= 0, target * capacity + rank, -1)
    picker = (place[:, None] == jnp.arange(number * capacity, dtype=jnp.int32)[None, :]).astype(
        jnp.bfloat16
    )
    packed = jnp.dot(picker.T, rows, preferred_element_type=jnp.float32).astype(jnp.bfloat16)
    labels = (
        jnp.sum(picker.T.astype(jnp.float32) * (local + 1).astype(jnp.float32)[None, :], axis=1)
        - 1.0
    )
    width = rows.shape[1]
    return (
        packed.reshape(number, capacity * width),
        labels.reshape(number, capacity),
    )


def pick(labels, streams):
    target = lax.broadcasted_iota(jnp.int32, (streams, labels.shape[1]), 0).astype(jnp.float32)
    return (target == labels).astype(jnp.bfloat16)


def conv_kernel(
    cache_ref, crecv_ref, precv_ref, klab_ref, clab_ref, plab_ref, uw_ref, w_ref, b_ref,
    lim_ref, o_ref, nc_ref, ext_ref,
):
    taps = w_ref.shape[0]
    streams, steps, block = o_ref.shape
    rows, _, channels = ext_ref.shape
    kept_rows = cache_ref.shape[0]
    frames = precv_ref.shape[1] // channels
    lim = lim_ref[...]

    @pl.when(pl.program_id(0) == 0)
    def _():
        keep_pick = pick(klab_ref[...], streams)
        cache_pick = pick(clab_ref[...], streams)
        panel_pick = pick(plab_ref[...], streams)

        def owned(row):
            here = jnp.dot(keep_pick, cache_ref[row], preferred_element_type=jnp.float32)
            came = jnp.dot(
                cache_pick,
                crecv_ref[:, row * channels : (row + 1) * channels],
                preferred_element_type=jnp.float32,
            )
            return (here + came).astype(ext_ref.dtype)

        prev = [owned(0)] + [
            jnp.dot(
                panel_pick,
                precv_ref[:, f * channels : (f + 1) * channels],
                preferred_element_type=jnp.float32,
            ).astype(ext_ref.dtype)
            for f in range(frames)
        ]
        for row in range(kept_rows - 1):
            ext_ref[row] = owned(row + 1)
        weight = uw_ref[...]
        for f in range(frames):
            current = prev[f + 1].astype(jnp.float32)
            earlier = prev[f].astype(jnp.float32)
            for j in range(2):
                value = weight[j : j + 1] * current + weight[j + 2 : j + 3] * earlier
                ext_ref[kept_rows - 1 + 2 * f + j] = value.astype(ext_ref.dtype)
        first = prev[1]
        tail = [ext_ref[2 + i] for i in range(kept_rows - 1)]
        for valid in range(2, frames + 1):
            chosen = lim == 2 * valid
            first = jnp.where(chosen, prev[valid], first)
            tail = [
                jnp.where(chosen, ext_ref[2 * valid + i], tail[i]) for i in range(kept_rows - 1)
            ]
        nc_ref[0] = first
        for i in range(kept_rows - 1):
            nc_ref[i + 1] = tail[i]

    acc = None
    for tap in range(taps):
        window = ext_ref[tap : tap + steps].reshape(steps * streams, channels)
        part = jnp.dot(window, w_ref[tap], preferred_element_type=jnp.float32)
        acc = part if acc is None else acc + part
    acc = acc + b_ref[...]
    act = jnp.where(acc > 0, acc, jnp.exp(jnp.minimum(acc, 0.0)) - 1.0)
    act = act.reshape(steps, streams, block)
    for step in range(steps):
        o_ref[:, step, :] = jnp.where(step < lim, act[step], 0.0).astype(o_ref.dtype)


def conv_call(cache_t, crecv, precv, klab, clab, plab, up_weight, conv_weight, conv_bias, limit, steps):
    kept_rows, streams, channels = cache_t.shape
    taps, _, outward = conv_weight.shape
    rows = kept_rows - 1 + steps
    block = 256 if outward % 256 == 0 else outward
    whole = lambda n: (0, 0)
    operands = (cache_t, crecv, precv, klab, clab, plab, up_weight)
    in_specs = [pl.BlockSpec(cache_t.shape, lambda n: (0, 0, 0))] + [
        pl.BlockSpec(x.shape, whole) for x in operands[1:]
    ]
    return pl.pallas_call(
        conv_kernel,
        out_shape=(
            jax.ShapeDtypeStruct((streams, steps, outward), jnp.bfloat16),
            jax.ShapeDtypeStruct(cache_t.shape, jnp.bfloat16),
        ),
        grid=(outward // block,),
        in_specs=in_specs
        + [
            pl.BlockSpec((taps, channels, block), lambda n: (0, 0, n)),
            pl.BlockSpec((1, block), lambda n: (0, n)),
            pl.BlockSpec((streams, 1), whole),
        ],
        out_specs=(
            pl.BlockSpec((streams, steps, block), lambda n: (0, 0, n)),
            pl.BlockSpec(cache_t.shape, lambda n: (0, 0, 0)),
        ),
        scratch_shapes=[pltpu.VMEM((rows, streams, channels), jnp.bfloat16)],
        compiler_params=pltpu.CompilerParams(dimension_semantics=("arbitrary",)),
    )(*operands, conv_weight, conv_bias.reshape(1, outward), limit)


def padded(rows, labels):
    extra = -rows.shape[0] % 128
    rows = jnp.pad(rows, ((0, extra), (0, 0)))
    labels = jnp.pad(labels, (0, extra), constant_values=-1.0)
    return rows, labels.reshape(1, -1)


def body(latents, cache, panel_slot, cache_slot, frames_valid, up_weight, conv_weight, conv_bias):
    number = lax.axis_size("dec")
    myself = lax.axis_index("dec")
    streams = latents.shape[0]
    frames = latents.shape[1]
    channels = latents.shape[2]
    rows_kept = cache.shape[1]
    pair_cap = max(2, (streams + number - 2) // (number - 1))
    mig_cap = max(2, (streams // 2 + number - 3) // (number - 2))
    panel_width = frames * channels
    cache_width = rows_kept * channels
    flat_latents = latents.reshape(streams, panel_width)
    flat_cache = cache.reshape(streams, cache_width)
    panel_owner = panel_slot // streams
    panel_local = panel_slot % streams
    cache_owner = cache_slot // streams
    cache_local = cache_slot % streams
    moving = cache_owner != myself
    staying = jnp.logical_not(moving)
    keep_labels = jnp.where(staying, cache_local, -1).astype(jnp.float32).reshape(1, streams)
    cache_send, cache_labels = buckets(
        flat_cache, jnp.where(moving, cache_owner, -1), cache_local, mig_cap, number
    )
    panel_send, panel_labels = buckets(flat_latents, panel_owner, panel_local, pair_cap, number)
    lane = LABEL_WIDTH
    panel_rows = pair_cap * panel_width // lane
    cache_rows = mig_cap * cache_width // lane
    label_rows = -(panel_rows + cache_rows + 1) % 16 + 1
    label_block = jnp.concatenate([panel_labels, cache_labels], axis=1)
    label_block = jnp.pad(
        label_block, ((0, 0), (0, label_rows * lane - label_block.shape[1])), constant_values=-1.0
    ).astype(jnp.bfloat16)
    joint = jnp.concatenate(
        [
            panel_send.reshape(number, panel_rows, lane),
            cache_send.reshape(number, cache_rows, lane),
            label_block.reshape(number, label_rows, lane),
        ],
        axis=1,
    )
    joint_recv = lax.all_to_all(joint, "dec", split_axis=0, concat_axis=0, tiled=True)
    panel_recv = joint_recv[:, :panel_rows].reshape(number * pair_cap, panel_width)
    cache_recv = joint_recv[:, panel_rows : panel_rows + cache_rows].reshape(
        number * mig_cap, cache_width
    )
    recv_labels = joint_recv[:, panel_rows + cache_rows, :].astype(jnp.float32)
    panel_rl = recv_labels[:, :pair_cap].reshape(-1)
    cache_rl = recv_labels[:, pair_cap : pair_cap + mig_cap].reshape(-1)
    precv, plab = padded(panel_recv, panel_rl)
    crecv, clab = padded(cache_recv, cache_rl)
    limit = (2 * frames_valid).reshape(streams, 1)
    cache_t = jnp.transpose(cache, (1, 0, 2))
    decoded, new_cache = conv_call(
        cache_t, crecv, precv, keep_labels, clab, plab, up_weight, conv_weight, conv_bias,
        limit, 2 * frames,
    )
    new_cache = jnp.transpose(new_cache, (1, 0, 2))
    return (decoded, new_cache)


def solution(mesh):
    in_specs = (
        P(("grp", "dec"), None, None),
        P(("grp", "dec"), None, None),
        P(("grp", "dec")),
        P(("grp", "dec")),
        P(("grp", "dec")),
        P(),
        P(),
        P(),
    )
    out_specs = (P(("grp", "dec"), None, None), P(("grp", "dec"), None, None))
    return jax.shard_map(body, mesh=mesh, in_specs=in_specs, out_specs=out_specs, check_vma=False)
```

```python
import jax
import jax.numpy as jnp
from jax import lax
from jax.experimental import pallas as pl
from jax.experimental.pallas import tpu as pltpu
from jax.sharding import PartitionSpec as P


LABEL_WIDTH = 128


def buckets(rows, target, local, capacity, number):
    hits = (target[:, None] == jnp.arange(number, dtype=jnp.int32)[None, :]).astype(jnp.int32)
    rank = jnp.sum(hits * (jnp.cumsum(hits, axis=0) - 1), axis=1)
    place = jnp.where(target >= 0, target * capacity + rank, -1)
    picker = (place[:, None] == jnp.arange(number * capacity, dtype=jnp.int32)[None, :]).astype(
        jnp.bfloat16
    )
    packed = jnp.dot(picker.T, rows, preferred_element_type=jnp.float32).astype(jnp.bfloat16)
    labels = (
        jnp.sum(picker.T.astype(jnp.float32) * (local + 1).astype(jnp.float32)[None, :], axis=1)
        - 1.0
    )
    width = rows.shape[1]
    return (
        packed.reshape(number, capacity * width),
        labels.reshape(number, capacity),
    )


def pick(labels, streams):
    target = lax.broadcasted_iota(jnp.int32, (streams, labels.shape[1]), 0).astype(jnp.float32)
    return (target == labels).astype(jnp.bfloat16)


def conv_kernel(
    cache_ref, crecv_ref, precv_ref, klab_ref, clab_ref, plab_ref, uw_ref, w_ref, b_ref,
    lim_ref, o_ref, nc_ref, ext_ref,
):
    taps = w_ref.shape[0]
    streams, steps, block = o_ref.shape
    rows, _, channels = ext_ref.shape
    kept_rows = cache_ref.shape[0]
    frames = precv_ref.shape[1] // channels
    lim = lim_ref[...]

    @pl.when(pl.program_id(0) == 0)
    def _():
        keep_pick = pick(klab_ref[...], streams)
        cache_pick = pick(clab_ref[...], streams)
        panel_pick = pick(plab_ref[...], streams)

        def owned(row):
            here = jnp.dot(keep_pick, cache_ref[row], preferred_element_type=jnp.float32)
            came = jnp.dot(
                cache_pick,
                crecv_ref[:, row * channels : (row + 1) * channels],
                preferred_element_type=jnp.float32,
            )
            return (here + came).astype(ext_ref.dtype)

        prev = [owned(0)] + [
            jnp.dot(
                panel_pick,
                precv_ref[:, f * channels : (f + 1) * channels],
                preferred_element_type=jnp.float32,
            ).astype(ext_ref.dtype)
            for f in range(frames)
        ]
        for row in range(kept_rows - 1):
            ext_ref[row] = owned(row + 1)
        weight = uw_ref[...]
        for f in range(frames):
            current = prev[f + 1].astype(jnp.float32)
            earlier = prev[f].astype(jnp.float32)
            for j in range(2):
                value = weight[j : j + 1] * current + weight[j + 2 : j + 3] * earlier
                ext_ref[kept_rows - 1 + 2 * f + j] = value.astype(ext_ref.dtype)
        first = prev[1]
        tail = [ext_ref[2 + i] for i in range(kept_rows - 1)]
        for valid in range(2, frames + 1):
            chosen = lim == 2 * valid
            first = jnp.where(chosen, prev[valid], first)
            tail = [
                jnp.where(chosen, ext_ref[2 * valid + i], tail[i]) for i in range(kept_rows - 1)
            ]
        nc_ref[0] = first
        for i in range(kept_rows - 1):
            nc_ref[i + 1] = tail[i]

    acc = None
    for tap in range(taps):
        window = ext_ref[tap : tap + steps].reshape(steps * streams, channels)
        part = jnp.dot(window, w_ref[tap], preferred_element_type=jnp.float32)
        acc = part if acc is None else acc + part
    acc = acc + b_ref[...]
    act = jnp.where(acc > 0, acc, jnp.exp(jnp.minimum(acc, 0.0)) - 1.0)
    act = act.reshape(steps, streams, block)
    for step in range(steps):
        o_ref[:, step, :] = jnp.where(step < lim, act[step], 0.0).astype(o_ref.dtype)


def conv_call(cache_t, crecv, precv, klab, clab, plab, up_weight, conv_weight, conv_bias, limit, steps):
    kept_rows, streams, channels = cache_t.shape
    taps, _, outward = conv_weight.shape
    rows = kept_rows - 1 + steps
    block = 256 if outward % 256 == 0 else outward
    whole = lambda n: (0, 0)
    operands = (cache_t, crecv, precv, klab, clab, plab, up_weight)
    in_specs = [pl.BlockSpec(cache_t.shape, lambda n: (0, 0, 0))] + [
        pl.BlockSpec(x.shape, whole) for x in operands[1:]
    ]
    return pl.pallas_call(
        conv_kernel,
        out_shape=(
            jax.ShapeDtypeStruct((streams, steps, outward), jnp.bfloat16),
            jax.ShapeDtypeStruct(cache_t.shape, jnp.bfloat16),
        ),
        grid=(outward // block,),
        in_specs=in_specs
        + [
            pl.BlockSpec((taps, channels, block), lambda n: (0, 0, n)),
            pl.BlockSpec((1, block), lambda n: (0, n)),
            pl.BlockSpec((streams, 1), whole),
        ],
        out_specs=(
            pl.BlockSpec((streams, steps, block), lambda n: (0, 0, n)),
            pl.BlockSpec(cache_t.shape, lambda n: (0, 0, 0)),
        ),
        scratch_shapes=[pltpu.VMEM((rows, streams, channels), jnp.bfloat16)],
        compiler_params=pltpu.CompilerParams(dimension_semantics=("arbitrary",)),
    )(*operands, conv_weight, conv_bias.reshape(1, outward), limit)


def padded(rows, labels):
    return rows, labels.reshape(1, -1)


def body(latents, cache, panel_slot, cache_slot, frames_valid, up_weight, conv_weight, conv_bias):
    number = lax.axis_size("dec")
    myself = lax.axis_index("dec")
    streams = latents.shape[0]
    frames = latents.shape[1]
    channels = latents.shape[2]
    rows_kept = cache.shape[1]
    pair_cap = max(2, (streams + number - 2) // (number - 1))
    mig_cap = max(2, (streams // 2 + number - 3) // (number - 2))
    panel_width = frames * channels
    cache_width = rows_kept * channels
    flat_latents = latents.reshape(streams, panel_width)
    flat_cache = cache.reshape(streams, cache_width)
    panel_owner = panel_slot // streams
    panel_local = panel_slot % streams
    cache_owner = cache_slot // streams
    cache_local = cache_slot % streams
    moving = cache_owner != myself
    staying = jnp.logical_not(moving)
    keep_labels = jnp.where(staying, cache_local, -1).astype(jnp.float32).reshape(1, streams)
    cache_send, cache_labels = buckets(
        flat_cache, jnp.where(moving, cache_owner, -1), cache_local, mig_cap, number
    )
    panel_send, panel_labels = buckets(flat_latents, panel_owner, panel_local, pair_cap, number)
    lane = LABEL_WIDTH
    panel_rows = pair_cap * panel_width // lane
    cache_rows = mig_cap * cache_width // lane
    label_rows = -(panel_rows + cache_rows + 1) % 16 + 1
    label_block = jnp.concatenate([panel_labels, cache_labels], axis=1)
    label_block = jnp.pad(
        label_block, ((0, 0), (0, label_rows * lane - label_block.shape[1])), constant_values=-1.0
    ).astype(jnp.bfloat16)
    joint = jnp.concatenate(
        [
            panel_send.reshape(number, panel_rows, lane),
            cache_send.reshape(number, cache_rows, lane),
            label_block.reshape(number, label_rows, lane),
        ],
        axis=1,
    )
    joint_recv = lax.all_to_all(joint, "dec", split_axis=0, concat_axis=0, tiled=True)
    panel_recv = joint_recv[:, :panel_rows].reshape(number * pair_cap, panel_width)
    cache_recv = joint_recv[:, panel_rows : panel_rows + cache_rows].reshape(
        number * mig_cap, cache_width
    )
    recv_labels = joint_recv[:, panel_rows + cache_rows, :].astype(jnp.float32)
    panel_rl = recv_labels[:, :pair_cap].reshape(-1)
    cache_rl = recv_labels[:, pair_cap : pair_cap + mig_cap].reshape(-1)
    precv, plab = padded(panel_recv, panel_rl)
    crecv, clab = padded(cache_recv, cache_rl)
    limit = (2 * frames_valid).reshape(streams, 1)
    cache_t = jnp.transpose(cache, (1, 0, 2))
    decoded, new_cache = conv_call(
        cache_t, crecv, precv, keep_labels, clab, plab, up_weight, conv_weight, conv_bias,
        limit, 2 * frames,
    )
    new_cache = jnp.transpose(new_cache, (1, 0, 2))
    return (decoded, new_cache)


def solution(mesh):
    in_specs = (
        P(("grp", "dec"), None, None),
        P(("grp", "dec"), None, None),
        P(("grp", "dec")),
        P(("grp", "dec")),
        P(("grp", "dec")),
        P(),
        P(),
        P(),
    )
    out_specs = (P(("grp", "dec"), None, None), P(("grp", "dec"), None, None))
    return jax.shard_map(body, mesh=mesh, in_specs=in_specs, out_specs=out_specs, check_vma=False)
```

```python
import jax
import jax.numpy as jnp
from jax import lax
from jax.experimental import pallas as pl
from jax.experimental.pallas import tpu as pltpu
from jax.sharding import PartitionSpec as P


LABEL_WIDTH = 128


def buckets(rows, target, local, capacity, number):
    count = target.shape[0]
    line = lax.broadcasted_iota(jnp.int32, (count, count), 0)
    column = lax.broadcasted_iota(jnp.int32, (count, count), 1)
    rank = jnp.sum(((target[None, :] == target[:, None]) & (column < line)).astype(jnp.int32), axis=1)
    place = jnp.where(target >= 0, target * capacity + rank, -1)
    picker = (place[:, None] == jnp.arange(number * capacity, dtype=jnp.int32)[None, :]).astype(
        jnp.bfloat16
    )
    packed = jnp.dot(picker.T, rows, preferred_element_type=jnp.float32).astype(jnp.bfloat16)
    labels = (
        jnp.sum(picker.T.astype(jnp.float32) * (local + 1).astype(jnp.float32)[None, :], axis=1)
        - 1.0
    )
    width = rows.shape[1]
    return (
        packed.reshape(number, capacity * width),
        labels.reshape(number, capacity),
    )


def settle(received, labels, streams):
    picker = (labels[:, None] == jnp.arange(streams, dtype=jnp.float32)[None, :]).astype(
        jnp.bfloat16
    )
    return jnp.dot(picker.T, received, preferred_element_type=jnp.float32)


def conv_kernel(own_ref, pan_ref, uw_ref, w_ref, b_ref, lim_ref, o_ref, nc_ref, ext_ref):
    taps = w_ref.shape[0]
    streams, steps, block = o_ref.shape
    rows, _, channels = ext_ref.shape
    kept_rows = own_ref.shape[1] // channels
    frames = pan_ref.shape[1] // channels
    lim = lim_ref[...]

    @pl.when(pl.program_id(0) == 0)
    def _():
        prev = [own_ref[:, 0:channels]] + [
            pan_ref[:, f * channels : (f + 1) * channels] for f in range(frames)
        ]
        for row in range(kept_rows - 1):
            ext_ref[row] = own_ref[:, (row + 1) * channels : (row + 2) * channels]
        weight = uw_ref[...]
        for f in range(frames):
            current = prev[f + 1].astype(jnp.float32)
            earlier = prev[f].astype(jnp.float32)
            for j in range(2):
                value = weight[j : j + 1] * current + weight[j + 2 : j + 3] * earlier
                ext_ref[kept_rows - 1 + 2 * f + j] = value.astype(ext_ref.dtype)
        first = prev[1]
        tail = [ext_ref[2 + i] for i in range(kept_rows - 1)]
        for valid in range(2, frames + 1):
            chosen = lim == 2 * valid
            first = jnp.where(chosen, prev[valid], first)
            tail = [
                jnp.where(chosen, ext_ref[2 * valid + i], tail[i]) for i in range(kept_rows - 1)
            ]
        nc_ref[0] = first
        for i in range(kept_rows - 1):
            nc_ref[i + 1] = tail[i]

    acc = None
    for tap in range(taps):
        window = ext_ref[tap : tap + steps].reshape(steps * streams, channels)
        part = jnp.dot(window, w_ref[tap], preferred_element_type=jnp.float32)
        acc = part if acc is None else acc + part
    acc = acc + b_ref[...]
    act = jnp.where(acc > 0, acc, jnp.exp(jnp.minimum(acc, 0.0)) - 1.0)
    act = act.reshape(steps, streams, block)
    for step in range(steps):
        o_ref[:, step, :] = jnp.where(step < lim, act[step], 0.0).astype(o_ref.dtype)


def conv_call(owned, panels, up_weight, conv_weight, conv_bias, limit, steps):
    streams, cache_width = owned.shape
    panel_width = panels.shape[1]
    taps, channels, outward = conv_weight.shape
    rows = cache_width // channels - 1 + steps
    block = 256 if outward % 256 == 0 else outward
    whole = lambda n: (0, 0)
    return pl.pallas_call(
        conv_kernel,
        out_shape=(
            jax.ShapeDtypeStruct((streams, steps, outward), jnp.bfloat16),
            jax.ShapeDtypeStruct((cache_width // channels, streams, channels), jnp.bfloat16),
        ),
        grid=(outward // block,),
        in_specs=[
            pl.BlockSpec((streams, cache_width), whole),
            pl.BlockSpec((streams, panel_width), whole),
            pl.BlockSpec(up_weight.shape, whole),
            pl.BlockSpec((taps, channels, block), lambda n: (0, 0, n)),
            pl.BlockSpec((1, block), lambda n: (0, n)),
            pl.BlockSpec((streams, 1), whole),
        ],
        out_specs=(
            pl.BlockSpec((streams, steps, block), lambda n: (0, 0, n)),
            pl.BlockSpec((cache_width // channels, streams, channels), lambda n: (0, 0, 0)),
        ),
        scratch_shapes=[pltpu.VMEM((rows, streams, channels), jnp.bfloat16)],
        compiler_params=pltpu.CompilerParams(dimension_semantics=("arbitrary",)),
    )(owned, panels, up_weight, conv_weight, conv_bias.reshape(1, outward), limit)


def body(latents, cache, panel_slot, cache_slot, frames_valid, up_weight, conv_weight, conv_bias):
    number = lax.axis_size("dec")
    myself = lax.axis_index("dec")
    streams = latents.shape[0]
    frames = latents.shape[1]
    channels = latents.shape[2]
    rows_kept = cache.shape[1]
    pair_cap = max(2, (streams + number - 2) // (number - 1))
    mig_cap = max(2, (streams // 2 + number - 3) // (number - 2))
    panel_width = frames * channels
    cache_width = rows_kept * channels
    flat_latents = latents.reshape(streams, panel_width)
    flat_cache = cache.reshape(streams, cache_width)
    panel_owner = lax.div(panel_slot, streams)
    panel_local = lax.rem(panel_slot, streams)
    cache_owner = lax.div(cache_slot, streams)
    cache_local = lax.rem(cache_slot, streams)
    moving = cache_owner != myself
    staying = jnp.logical_not(moving)
    stay_pick = (
        staying[:, None] & (cache_local[:, None] == jnp.arange(streams, dtype=jnp.int32)[None, :])
    ).astype(jnp.bfloat16)
    kept = jnp.dot(stay_pick.T, flat_cache, preferred_element_type=jnp.float32)
    cache_send, cache_labels = buckets(
        flat_cache, jnp.where(moving, cache_owner, -1), cache_local, mig_cap, number
    )
    panel_send, panel_labels = buckets(flat_latents, panel_owner, panel_local, pair_cap, number)
    lane = LABEL_WIDTH
    panel_rows = pair_cap * panel_width // lane
    cache_rows = mig_cap * cache_width // lane
    label_rows = -(panel_rows + cache_rows + 1) % 16 + 1
    label_block = jnp.concatenate([panel_labels, cache_labels], axis=1)
    label_block = jnp.pad(
        label_block, ((0, 0), (0, label_rows * lane - label_block.shape[1])), constant_values=-1.0
    ).astype(jnp.bfloat16)
    joint = jnp.concatenate(
        [
            panel_send.reshape(number, panel_rows, lane),
            cache_send.reshape(number, cache_rows, lane),
            label_block.reshape(number, label_rows, lane),
        ],
        axis=1,
    )
    joint_recv = lax.all_to_all(joint, "dec", split_axis=0, concat_axis=0, tiled=True)
    panel_recv = joint_recv[:, :panel_rows].reshape(number * pair_cap, panel_width)
    cache_recv = joint_recv[:, panel_rows : panel_rows + cache_rows].reshape(
        number * mig_cap, cache_width
    )
    recv_labels = joint_recv[:, panel_rows + cache_rows, :].astype(jnp.float32)
    panel_rl = recv_labels[:, :pair_cap].reshape(-1)
    cache_rl = recv_labels[:, pair_cap : pair_cap + mig_cap].reshape(-1)
    panels = settle(panel_recv, panel_rl, streams).astype(jnp.bfloat16)
    arrived = settle(cache_recv, cache_rl, streams)
    owned = (kept + arrived).astype(jnp.bfloat16)
    limit = (2 * frames_valid).reshape(streams, 1)
    decoded, new_cache = conv_call(
        owned, panels, up_weight, conv_weight, conv_bias, limit, 2 * frames
    )
    new_cache = jnp.transpose(new_cache, (1, 0, 2))
    return (decoded, new_cache)


def solution(mesh):
    in_specs = (
        P(("grp", "dec"), None, None),
        P(("grp", "dec"), None, None),
        P(("grp", "dec")),
        P(("grp", "dec")),
        P(("grp", "dec")),
        P(),
        P(),
        P(),
    )
    out_specs = (P(("grp", "dec"), None, None), P(("grp", "dec"), None, None))
    return jax.shard_map(body, mesh=mesh, in_specs=in_specs, out_specs=out_specs, check_vma=False)
```

```python
import jax
import jax.numpy as jnp
from jax import lax
from jax.experimental import pallas as pl
from jax.experimental.pallas import tpu as pltpu
from jax.sharding import PartitionSpec as P


LABEL_WIDTH = 128


def buckets(rows, target, local, capacity, number):
    count = target.shape[0]
    line = lax.broadcasted_iota(jnp.int32, (count, count), 0)
    column = lax.broadcasted_iota(jnp.int32, (count, count), 1)
    rank = jnp.sum(((target[None, :] == target[:, None]) & (column < line)).astype(jnp.int32), axis=1)
    place = jnp.where(target >= 0, target * capacity + rank, -1)
    picker = (place[:, None] == jnp.arange(number * capacity, dtype=jnp.int32)[None, :]).astype(
        jnp.bfloat16
    )
    packed = jnp.dot(picker.T, rows, preferred_element_type=jnp.float32).astype(jnp.bfloat16)
    labels = (
        jnp.sum(picker.T.astype(jnp.float32) * (local + 1).astype(jnp.float32)[None, :], axis=1)
        - 1.0
    )
    width = rows.shape[1]
    return (
        packed.reshape(number, capacity * width),
        labels.reshape(number, capacity),
    )


def settle(received, labels, streams):
    picker = (labels[:, None] == jnp.arange(streams, dtype=jnp.float32)[None, :]).astype(
        jnp.bfloat16
    )
    return jnp.dot(picker.T, received, preferred_element_type=jnp.float32)


def conv_kernel(own_ref, pan_ref, uw_ref, w_ref, b_ref, lim_ref, o_ref, nc_ref, ext_ref):
    taps = w_ref.shape[0]
    streams, steps, block = o_ref.shape
    rows, _, channels = ext_ref.shape
    kept_rows = own_ref.shape[1] // channels
    frames = pan_ref.shape[1] // channels
    lim = lim_ref[...]

    @pl.when(pl.program_id(0) == 0)
    def _():
        prev = [own_ref[:, 0:channels]] + [
            pan_ref[:, f * channels : (f + 1) * channels] for f in range(frames)
        ]
        for row in range(kept_rows - 1):
            ext_ref[row] = own_ref[:, (row + 1) * channels : (row + 2) * channels]
        weight = uw_ref[...]
        for f in range(frames):
            current = prev[f + 1].astype(jnp.float32)
            earlier = prev[f].astype(jnp.float32)
            for j in range(2):
                value = weight[j : j + 1] * current + weight[j + 2 : j + 3] * earlier
                ext_ref[kept_rows - 1 + 2 * f + j] = value.astype(ext_ref.dtype)
        first = prev[1]
        tail = [ext_ref[2 + i] for i in range(kept_rows - 1)]
        for valid in range(2, frames + 1):
            chosen = lim == 2 * valid
            first = jnp.where(chosen, prev[valid], first)
            tail = [
                jnp.where(chosen, ext_ref[2 * valid + i], tail[i]) for i in range(kept_rows - 1)
            ]
        nc_ref[0] = first
        for i in range(kept_rows - 1):
            nc_ref[i + 1] = tail[i]

    acc = None
    for tap in range(taps):
        window = ext_ref[tap : tap + steps].reshape(steps * streams, channels)
        part = jnp.dot(window, w_ref[tap], preferred_element_type=jnp.float32)
        acc = part if acc is None else acc + part
    acc = acc + b_ref[...]
    act = jnp.where(acc > 0, acc, jnp.exp(acc) - 1.0)
    act = act.reshape(steps, streams, block)
    for step in range(steps):
        o_ref[:, step, :] = jnp.where(step < lim, act[step], 0.0).astype(o_ref.dtype)


def conv_call(owned, panels, up_weight, conv_weight, conv_bias, limit, steps):
    streams, cache_width = owned.shape
    panel_width = panels.shape[1]
    taps, channels, outward = conv_weight.shape
    rows = cache_width // channels - 1 + steps
    block = 256 if outward % 256 == 0 else outward
    whole = lambda n: (0, 0)
    return pl.pallas_call(
        conv_kernel,
        out_shape=(
            jax.ShapeDtypeStruct((streams, steps, outward), jnp.bfloat16),
            jax.ShapeDtypeStruct((cache_width // channels, streams, channels), jnp.bfloat16),
        ),
        grid=(outward // block,),
        in_specs=[
            pl.BlockSpec((streams, cache_width), whole),
            pl.BlockSpec((streams, panel_width), whole),
            pl.BlockSpec(up_weight.shape, whole),
            pl.BlockSpec((taps, channels, block), lambda n: (0, 0, n)),
            pl.BlockSpec((1, block), lambda n: (0, n)),
            pl.BlockSpec((streams, 1), whole),
        ],
        out_specs=(
            pl.BlockSpec((streams, steps, block), lambda n: (0, 0, n)),
            pl.BlockSpec((cache_width // channels, streams, channels), lambda n: (0, 0, 0)),
        ),
        scratch_shapes=[pltpu.VMEM((rows, streams, channels), jnp.bfloat16)],
        compiler_params=pltpu.CompilerParams(dimension_semantics=("arbitrary",)),
    )(owned, panels, up_weight, conv_weight, conv_bias.reshape(1, outward), limit)


def body(latents, cache, panel_slot, cache_slot, frames_valid, up_weight, conv_weight, conv_bias):
    number = lax.axis_size("dec")
    myself = lax.axis_index("dec")
    streams = latents.shape[0]
    frames = latents.shape[1]
    channels = latents.shape[2]
    rows_kept = cache.shape[1]
    pair_cap = max(2, (streams + number - 2) // (number - 1))
    mig_cap = max(2, (streams // 2 + number - 3) // (number - 2))
    panel_width = frames * channels
    cache_width = rows_kept * channels
    flat_latents = latents.reshape(streams, panel_width)
    flat_cache = cache.reshape(streams, cache_width)
    panel_owner = lax.div(panel_slot, streams)
    panel_local = lax.rem(panel_slot, streams)
    cache_owner = lax.div(cache_slot, streams)
    cache_local = lax.rem(cache_slot, streams)
    moving = cache_owner != myself
    staying = jnp.logical_not(moving)
    stay_pick = (
        staying[:, None] & (cache_local[:, None] == jnp.arange(streams, dtype=jnp.int32)[None, :])
    ).astype(jnp.bfloat16)
    kept = lax.optimization_barrier(
        jnp.dot(stay_pick.T, flat_cache, preferred_element_type=jnp.float32).astype(jnp.bfloat16)
    )
    cache_send, cache_labels = buckets(
        flat_cache, jnp.where(moving, cache_owner, -1), cache_local, mig_cap, number
    )
    panel_send, panel_labels = buckets(flat_latents, panel_owner, panel_local, pair_cap, number)
    lane = LABEL_WIDTH
    panel_rows = pair_cap * panel_width // lane
    cache_rows = mig_cap * cache_width // lane
    label_rows = -(panel_rows + cache_rows + 1) % 16 + 1
    label_block = jnp.concatenate([panel_labels, cache_labels], axis=1)
    label_block = jnp.pad(
        label_block, ((0, 0), (0, label_rows * lane - label_block.shape[1])), constant_values=-1.0
    ).astype(jnp.bfloat16)
    joint = jnp.concatenate(
        [
            panel_send.reshape(number, panel_rows, lane),
            cache_send.reshape(number, cache_rows, lane),
            label_block.reshape(number, label_rows, lane),
        ],
        axis=1,
    )
    joint_recv = lax.all_to_all(joint, "dec", split_axis=0, concat_axis=0, tiled=True)
    panel_recv = joint_recv[:, :panel_rows].reshape(number * pair_cap, panel_width)
    cache_recv = joint_recv[:, panel_rows : panel_rows + cache_rows].reshape(
        number * mig_cap, cache_width
    )
    recv_labels = joint_recv[:, panel_rows + cache_rows, :].astype(jnp.float32)
    panel_rl = recv_labels[:, :pair_cap].reshape(-1)
    cache_rl = recv_labels[:, pair_cap : pair_cap + mig_cap].reshape(-1)
    panels = settle(panel_recv, panel_rl, streams).astype(jnp.bfloat16)
    arrived = settle(cache_recv, cache_rl, streams)
    owned = (kept.astype(jnp.float32) + arrived).astype(jnp.bfloat16)
    limit = (2 * frames_valid).reshape(streams, 1)
    decoded, new_cache = conv_call(
        owned, panels, up_weight, conv_weight, conv_bias, limit, 2 * frames
    )
    new_cache = jnp.transpose(new_cache, (1, 0, 2))
    return (decoded, new_cache)


def solution(mesh):
    in_specs = (
        P(("grp", "dec"), None, None),
        P(("grp", "dec"), None, None),
        P(("grp", "dec")),
        P(("grp", "dec")),
        P(("grp", "dec")),
        P(),
        P(),
        P(),
    )
    out_specs = (P(("grp", "dec"), None, None), P(("grp", "dec"), None, None))
    return jax.shard_map(body, mesh=mesh, in_specs=in_specs, out_specs=out_specs, check_vma=False)
```

```python
import jax
import jax.numpy as jnp
from jax import lax
from jax.experimental import pallas as pl
from jax.experimental.pallas import tpu as pltpu
from jax.sharding import PartitionSpec as P


LABEL_WIDTH = 128


def buckets(rows, target, local, capacity, number):
    count = target.shape[0]
    line = lax.broadcasted_iota(jnp.int32, (count, count), 0)
    column = lax.broadcasted_iota(jnp.int32, (count, count), 1)
    rank = jnp.sum(((target[None, :] == target[:, None]) & (column < line)).astype(jnp.int32), axis=1)
    place = jnp.where(target >= 0, target * capacity + rank, -1)
    picker = (place[:, None] == jnp.arange(number * capacity, dtype=jnp.int32)[None, :]).astype(
        jnp.bfloat16
    )
    packed = jnp.dot(picker.T, rows, preferred_element_type=jnp.float32).astype(jnp.bfloat16)
    labels = (
        jnp.sum(picker.T.astype(jnp.float32) * (local + 1).astype(jnp.float32)[None, :], axis=1)
        - 1.0
    )
    width = rows.shape[1]
    return (
        packed.reshape(number, capacity * width),
        labels.reshape(number, capacity),
    )


def settle(received, labels, streams):
    picker = (labels[:, None] == jnp.arange(streams, dtype=jnp.float32)[None, :]).astype(
        jnp.bfloat16
    )
    return jnp.dot(picker.T, received, preferred_element_type=jnp.float32)


def conv_kernel(own_ref, pan_ref, uw_ref, w_ref, b_ref, lim_ref, o_ref, nc_ref, ext_ref):
    taps = w_ref.shape[0]
    streams, steps, block = o_ref.shape
    rows, _, channels = ext_ref.shape
    kept_rows = own_ref.shape[1] // channels
    frames = pan_ref.shape[1] // channels
    lim = lim_ref[...]

    @pl.when(pl.program_id(0) == 0)
    def _():
        prev = [own_ref[:, 0:channels]] + [
            pan_ref[:, f * channels : (f + 1) * channels] for f in range(frames)
        ]
        for row in range(kept_rows - 1):
            ext_ref[row] = own_ref[:, (row + 1) * channels : (row + 2) * channels]
        weight = uw_ref[...]
        for f in range(frames):
            current = prev[f + 1].astype(jnp.float32)
            earlier = prev[f].astype(jnp.float32)
            for j in range(2):
                value = weight[j : j + 1] * current + weight[j + 2 : j + 3] * earlier
                ext_ref[kept_rows - 1 + 2 * f + j] = value.astype(ext_ref.dtype)
        first = prev[1]
        tail = [ext_ref[2 + i] for i in range(kept_rows - 1)]
        for valid in range(2, frames + 1):
            chosen = lim == 2 * valid
            first = jnp.where(chosen, prev[valid], first)
            tail = [
                jnp.where(chosen, ext_ref[2 * valid + i], tail[i]) for i in range(kept_rows - 1)
            ]
        nc_ref[0] = first
        for i in range(kept_rows - 1):
            nc_ref[i + 1] = tail[i]

    acc = None
    for tap in range(taps):
        window = ext_ref[tap : tap + steps].reshape(steps * streams, channels)
        part = jnp.dot(window, w_ref[tap], preferred_element_type=jnp.float32)
        acc = part if acc is None else acc + part
    acc = acc + b_ref[...]
    act = jnp.where(acc > 0, acc, jnp.exp(acc) - 1.0)
    act = act.reshape(steps, streams, block)
    for step in range(steps):
        o_ref[:, step, :] = jnp.where(step < lim, act[step], 0.0).astype(o_ref.dtype)


def conv_call(owned, panels, up_weight, conv_weight, conv_bias, limit, steps):
    streams, cache_width = owned.shape
    panel_width = panels.shape[1]
    taps, channels, outward = conv_weight.shape
    rows = cache_width // channels - 1 + steps
    block = 256 if outward % 256 == 0 else outward
    whole = lambda n: (0, 0)
    return pl.pallas_call(
        conv_kernel,
        out_shape=(
            jax.ShapeDtypeStruct((streams, steps, outward), jnp.bfloat16),
            jax.ShapeDtypeStruct((cache_width // channels, streams, channels), jnp.bfloat16),
        ),
        grid=(outward // block,),
        in_specs=[
            pl.BlockSpec((streams, cache_width), whole),
            pl.BlockSpec((streams, panel_width), whole),
            pl.BlockSpec(up_weight.shape, whole),
            pl.BlockSpec((taps, channels, block), lambda n: (0, 0, n)),
            pl.BlockSpec((1, block), lambda n: (0, n)),
            pl.BlockSpec((streams, 1), whole),
        ],
        out_specs=(
            pl.BlockSpec((streams, steps, block), lambda n: (0, 0, n)),
            pl.BlockSpec((cache_width // channels, streams, channels), lambda n: (0, 0, 0)),
        ),
        scratch_shapes=[pltpu.VMEM((rows, streams, channels), jnp.bfloat16)],
        compiler_params=pltpu.CompilerParams(dimension_semantics=("arbitrary",)),
    )(owned, panels, up_weight, conv_weight, conv_bias.reshape(1, outward), limit)


def body(latents, cache, panel_slot, cache_slot, frames_valid, up_weight, conv_weight, conv_bias):
    number = lax.axis_size("dec")
    myself = lax.axis_index("dec")
    streams = latents.shape[0]
    frames = latents.shape[1]
    channels = latents.shape[2]
    rows_kept = cache.shape[1]
    pair_cap = max(2, (streams + number - 2) // (number - 1))
    mig_cap = max(2, (streams // 2 + number - 3) // (number - 2))
    panel_width = frames * channels
    cache_width = rows_kept * channels
    flat_latents = latents.reshape(streams, panel_width)
    flat_cache = cache.reshape(streams, cache_width)
    slots = jnp.stack([panel_slot, cache_slot, frames_valid])
    owners = lax.div(slots, streams)
    locals_ = lax.rem(slots, streams)
    panel_owner, cache_owner = owners[0], owners[1]
    panel_local, cache_local = locals_[0], locals_[1]
    frames_valid = slots[2]
    moving = cache_owner != myself
    staying = jnp.logical_not(moving)
    stay_pick = (
        staying[:, None] & (cache_local[:, None] == jnp.arange(streams, dtype=jnp.int32)[None, :])
    ).astype(jnp.bfloat16)
    kept = lax.optimization_barrier(
        jnp.dot(stay_pick.T, flat_cache, preferred_element_type=jnp.float32).astype(jnp.bfloat16)
    )
    cache_send, cache_labels = buckets(
        flat_cache, jnp.where(moving, cache_owner, -1), cache_local, mig_cap, number
    )
    panel_send, panel_labels = buckets(flat_latents, panel_owner, panel_local, pair_cap, number)
    lane = LABEL_WIDTH
    panel_rows = pair_cap * panel_width // lane
    cache_rows = mig_cap * cache_width // lane
    label_rows = -(panel_rows + cache_rows + 1) % 16 + 1
    label_block = jnp.concatenate([panel_labels, cache_labels], axis=1)
    label_block = jnp.pad(
        label_block, ((0, 0), (0, label_rows * lane - label_block.shape[1])), constant_values=-1.0
    ).astype(jnp.bfloat16)
    joint = jnp.concatenate(
        [
            panel_send.reshape(number, panel_rows, lane),
            cache_send.reshape(number, cache_rows, lane),
            label_block.reshape(number, label_rows, lane),
        ],
        axis=1,
    )
    joint_recv = lax.all_to_all(joint, "dec", split_axis=0, concat_axis=0, tiled=True)
    panel_recv = joint_recv[:, :panel_rows].reshape(number * pair_cap, panel_width)
    cache_recv = joint_recv[:, panel_rows : panel_rows + cache_rows].reshape(
        number * mig_cap, cache_width
    )
    recv_labels = joint_recv[:, panel_rows + cache_rows, :].astype(jnp.float32)
    panel_rl = recv_labels[:, :pair_cap].reshape(-1)
    cache_rl = recv_labels[:, pair_cap : pair_cap + mig_cap].reshape(-1)
    panels = settle(panel_recv, panel_rl, streams).astype(jnp.bfloat16)
    arrived = settle(cache_recv, cache_rl, streams)
    owned = (kept.astype(jnp.float32) + arrived).astype(jnp.bfloat16)
    limit = (2 * frames_valid).reshape(streams, 1)
    decoded, new_cache = conv_call(
        owned, panels, up_weight, conv_weight, conv_bias, limit, 2 * frames
    )
    new_cache = jnp.transpose(new_cache, (1, 0, 2))
    return (decoded, new_cache)


def solution(mesh):
    in_specs = (
        P(("grp", "dec"), None, None),
        P(("grp", "dec"), None, None),
        P(("grp", "dec")),
        P(("grp", "dec")),
        P(("grp", "dec")),
        P(),
        P(),
        P(),
    )
    out_specs = (P(("grp", "dec"), None, None), P(("grp", "dec"), None, None))
    return jax.shard_map(body, mesh=mesh, in_specs=in_specs, out_specs=out_specs, check_vma=False)
```

```python
import jax
import jax.numpy as jnp
from jax import lax
from jax.experimental import pallas as pl
from jax.experimental.pallas import tpu as pltpu
from jax.sharding import PartitionSpec as P


LABEL_WIDTH = 128


def buckets(rows, target, local, capacity, number):
    count = target.shape[0]
    line = lax.broadcasted_iota(jnp.int32, (count, count), 0)
    column = lax.broadcasted_iota(jnp.int32, (count, count), 1)
    rank = jnp.sum(((target[None, :] == target[:, None]) & (column < line)).astype(jnp.int32), axis=1)
    place = jnp.where(target >= 0, target * capacity + rank, -1)
    picker = (place[:, None] == jnp.arange(number * capacity, dtype=jnp.int32)[None, :]).astype(
        jnp.bfloat16
    )
    packed = jnp.dot(picker.T, rows, preferred_element_type=jnp.float32).astype(jnp.bfloat16)
    labels = (
        jnp.sum(picker.T.astype(jnp.float32) * (local + 1).astype(jnp.float32)[None, :], axis=1)
        - 1.0
    )
    width = rows.shape[1]
    return (
        packed.reshape(number, capacity * width),
        labels.reshape(number, capacity),
    )


def settle(received, labels, streams):
    picker = (labels[:, None] == jnp.arange(streams, dtype=jnp.float32)[None, :]).astype(
        jnp.bfloat16
    )
    return jnp.dot(picker.T, received, preferred_element_type=jnp.float32)


def conv_kernel(own_ref, pan_ref, uw_ref, w_ref, b_ref, lim_ref, o_ref, nc_ref, ext_ref, out_ref):
    taps = w_ref.shape[0]
    streams, steps, block = o_ref.shape
    rows, _, channels = ext_ref.shape
    kept_rows = own_ref.shape[1] // channels
    frames = pan_ref.shape[1] // channels
    lim = lim_ref[...]

    @pl.when(pl.program_id(0) == 0)
    def _():
        prev = [own_ref[:, 0:channels]] + [
            pan_ref[:, f * channels : (f + 1) * channels] for f in range(frames)
        ]
        for row in range(kept_rows - 1):
            ext_ref[row] = own_ref[:, (row + 1) * channels : (row + 2) * channels]
        weight = uw_ref[...]
        for f in range(frames):
            current = prev[f + 1].astype(jnp.float32)
            earlier = prev[f].astype(jnp.float32)
            for j in range(2):
                value = weight[j : j + 1] * current + weight[j + 2 : j + 3] * earlier
                ext_ref[kept_rows - 1 + 2 * f + j] = value.astype(ext_ref.dtype)
        first = prev[1]
        tail = [ext_ref[2 + i] for i in range(kept_rows - 1)]
        for valid in range(2, frames + 1):
            chosen = lim == 2 * valid
            first = jnp.where(chosen, prev[valid], first)
            tail = [
                jnp.where(chosen, ext_ref[2 * valid + i], tail[i]) for i in range(kept_rows - 1)
            ]
        nc_ref[0] = first
        for i in range(kept_rows - 1):
            nc_ref[i + 1] = tail[i]

    acc = None
    for tap in range(taps):
        window = ext_ref[tap : tap + steps].reshape(steps * streams, channels)
        part = jnp.dot(window, w_ref[tap], preferred_element_type=jnp.float32)
        acc = part if acc is None else acc + part
    acc = acc + b_ref[...]
    act = jnp.where(acc > 0, acc, jnp.exp(acc) - 1.0)
    act = act.reshape(steps, streams, block)
    for step in range(steps):
        out_ref[:, step, :] = jnp.where(step < lim, act[step], 0.0)
    o_ref[...] = out_ref[...].astype(o_ref.dtype)


def conv_call(owned, panels, up_weight, conv_weight, conv_bias, limit, steps):
    streams, cache_width = owned.shape
    panel_width = panels.shape[1]
    taps, channels, outward = conv_weight.shape
    rows = cache_width // channels - 1 + steps
    block = 256 if outward % 256 == 0 else outward
    whole = lambda n: (0, 0)
    return pl.pallas_call(
        conv_kernel,
        out_shape=(
            jax.ShapeDtypeStruct((streams, steps, outward), jnp.bfloat16),
            jax.ShapeDtypeStruct((cache_width // channels, streams, channels), jnp.bfloat16),
        ),
        grid=(outward // block,),
        in_specs=[
            pl.BlockSpec((streams, cache_width), whole),
            pl.BlockSpec((streams, panel_width), whole),
            pl.BlockSpec(up_weight.shape, whole),
            pl.BlockSpec((taps, channels, block), lambda n: (0, 0, n)),
            pl.BlockSpec((1, block), lambda n: (0, n)),
            pl.BlockSpec((streams, 1), whole),
        ],
        out_specs=(
            pl.BlockSpec((streams, steps, block), lambda n: (0, 0, n)),
            pl.BlockSpec((cache_width // channels, streams, channels), lambda n: (0, 0, 0)),
        ),
        scratch_shapes=[
            pltpu.VMEM((rows, streams, channels), jnp.bfloat16),
            pltpu.VMEM((streams, steps, block), jnp.float32),
        ],
        compiler_params=pltpu.CompilerParams(dimension_semantics=("arbitrary",)),
    )(owned, panels, up_weight, conv_weight, conv_bias.reshape(1, outward), limit)


def body(latents, cache, panel_slot, cache_slot, frames_valid, up_weight, conv_weight, conv_bias):
    number = lax.axis_size("dec")
    myself = lax.axis_index("dec")
    streams = latents.shape[0]
    frames = latents.shape[1]
    channels = latents.shape[2]
    rows_kept = cache.shape[1]
    pair_cap = max(2, (streams + number - 2) // (number - 1))
    mig_cap = max(2, (streams // 2 + number - 3) // (number - 2))
    panel_width = frames * channels
    cache_width = rows_kept * channels
    flat_latents = latents.reshape(streams, panel_width)
    flat_cache = cache.reshape(streams, cache_width)
    slots = jnp.stack([panel_slot, cache_slot, frames_valid])
    owners = lax.div(slots, streams)
    locals_ = lax.rem(slots, streams)
    panel_owner, cache_owner = owners[0], owners[1]
    panel_local, cache_local = locals_[0], locals_[1]
    frames_valid = slots[2]
    moving = cache_owner != myself
    staying = jnp.logical_not(moving)
    stay_pick = (
        staying[:, None] & (cache_local[:, None] == jnp.arange(streams, dtype=jnp.int32)[None, :])
    ).astype(jnp.bfloat16)
    kept = lax.optimization_barrier(
        jnp.dot(stay_pick.T, flat_cache, preferred_element_type=jnp.float32).astype(jnp.bfloat16)
    )
    cache_send, cache_labels = buckets(
        flat_cache, jnp.where(moving, cache_owner, -1), cache_local, mig_cap, number
    )
    panel_send, panel_labels = buckets(flat_latents, panel_owner, panel_local, pair_cap, number)
    lane = LABEL_WIDTH
    panel_rows = pair_cap * panel_width // lane
    cache_rows = mig_cap * cache_width // lane
    label_rows = -(panel_rows + cache_rows + 1) % 16 + 1
    label_block = jnp.concatenate([panel_labels, cache_labels], axis=1)
    label_block = jnp.pad(
        label_block, ((0, 0), (0, label_rows * lane - label_block.shape[1])), constant_values=-1.0
    ).astype(jnp.bfloat16)
    joint = jnp.concatenate(
        [
            panel_send.reshape(number, panel_rows, lane),
            cache_send.reshape(number, cache_rows, lane),
            label_block.reshape(number, label_rows, lane),
        ],
        axis=1,
    )
    joint_recv = lax.all_to_all(joint, "dec", split_axis=0, concat_axis=0, tiled=True)
    panel_recv = joint_recv[:, :panel_rows].reshape(number * pair_cap, panel_width)
    cache_recv = joint_recv[:, panel_rows : panel_rows + cache_rows].reshape(
        number * mig_cap, cache_width
    )
    recv_labels = joint_recv[:, panel_rows + cache_rows, :].astype(jnp.float32)
    panel_rl = recv_labels[:, :pair_cap].reshape(-1)
    cache_rl = recv_labels[:, pair_cap : pair_cap + mig_cap].reshape(-1)
    panels = settle(panel_recv, panel_rl, streams).astype(jnp.bfloat16)
    arrived = settle(cache_recv, cache_rl, streams)
    owned = (kept.astype(jnp.float32) + arrived).astype(jnp.bfloat16)
    limit = (2 * frames_valid).reshape(streams, 1)
    decoded, new_cache = conv_call(
        owned, panels, up_weight, conv_weight, conv_bias, limit, 2 * frames
    )
    new_cache = jnp.transpose(new_cache, (1, 0, 2))
    return (decoded, new_cache)


def solution(mesh):
    in_specs = (
        P(("grp", "dec"), None, None),
        P(("grp", "dec"), None, None),
        P(("grp", "dec")),
        P(("grp", "dec")),
        P(("grp", "dec")),
        P(),
        P(),
        P(),
    )
    out_specs = (P(("grp", "dec"), None, None), P(("grp", "dec"), None, None))
    return jax.shard_map(body, mesh=mesh, in_specs=in_specs, out_specs=out_specs, check_vma=False)
```
